32 devices in a mesh: ctx: 8 (over z, x), dp: 4 (over y, core).
Axes of the slice: x: 2, y: 2, z: 4, core: 2. Of those that a mesh axis runs over, the one named last changes fastest.
Arguments:
- query: bfloat16 [4, 4096, 2048], P('dp', 'ctx'), may hold values from -0.75 to 0.75
- keys: bfloat16 [4, 4096, 2048], P('dp', 'ctx'), may hold values from -0.75 to 0.75
- values: bfloat16 [4, 4096, 2048], P('dp', 'ctx'), may hold values from -6 to 6
- upstream: bfloat16 [4, 4096, 2048], P('dp', 'ctx'), may hold values from -0.75 to 0.75
- out_weight: bfloat16 [2048, 2048], replicated, may hold values from -0.125 to 0.125
- log_decay: float32 [4, 4096, 16], P('dp', 'ctx'), may hold values from -0.9 to 0, as said below
- signs: int32 [4, 4096], P('dp', 'ctx'), may hold values 0 or 1
- magnitude: float32 [4, 4096], P('dp', 'ctx'), may hold values from 0.5 to 2
Outputs:
- grad_query: bfloat16 [4, 4096, 2048], P('dp', 'ctx')
- grad_keys: bfloat16 [4, 4096, 2048], P('dp', 'ctx')
- grad_values: bfloat16 [4, 4096, 2048], P('dp', 'ctx')
- grad_out_weight: float32 [2048, 2048], P(('ctx', 'dp'))
The draws below stay inside these ranges and needn't reach their ends.
Inputs may be any that keep to these rules, and one draw needn't show every extreme that they name: `log_decay`: every entry is negative.
All inputs are finite; a program needn't handle non-finite values. No bound on the sum of `signs` on one device may be relied on, other than what follows from the above.
Results may differ from the reference program's by a relative error of at most 0.006.
Values sent between devices are 32-bit elements; how exact they have to be, the bound alone decides.
No kernel may reach another device: no remote copies, remote signals or barrier semaphores. Data moves between devices by JAX's collectives and lax.ppermute only.
A program may use at most 192 MiB of HBM per device.

```python
import math
import jax
import jax.numpy as jnp
from jax import lax

LOCAL_HEADS = 16
HD = 128
DM = 2048
TOK_DEV = 512
BLOCK = 512
ROLLOUT_LENGTH = 4096
ROLLOUT_COUNT = 4


def draw_log_decay(key, part):
    every_key_row = jax.random.split(key, 6)
    fast = jax.random.uniform(every_key_row[0], (LOCAL_HEADS,)) < 0.5
    fast_rate = jnp.exp(jax.random.uniform(every_key_row[1], (LOCAL_HEADS,), minval=math.log(1.0 / 50), maxval=math.log(1.0 / 30)))
    slow_rate = jnp.exp(jax.random.uniform(every_key_row[2], (LOCAL_HEADS,), minval=math.log(0.03 / ROLLOUT_LENGTH), maxval=math.log(0.3 / ROLLOUT_LENGTH)))
    decay_speed = jnp.where(fast, fast_rate, slow_rate)
    approximate_estimate = jnp.exp(jax.random.uniform(every_key_row[3], (ROLLOUT_COUNT, ROLLOUT_LENGTH, LOCAL_HEADS), minval=math.log(0.5), maxval=math.log(2.0)))
    machine_multiplier = jnp.exp(jax.random.uniform(every_key_row[4], (ROLLOUT_COUNT, ROLLOUT_LENGTH // TOK_DEV, 1, LOCAL_HEADS), minval=math.log(0.5), maxval=math.log(2.0)))
    machine_multiplier = jnp.broadcast_to(machine_multiplier, (ROLLOUT_COUNT, ROLLOUT_LENGTH // TOK_DEV, TOK_DEV, LOCAL_HEADS)).reshape(ROLLOUT_COUNT, ROLLOUT_LENGTH, LOCAL_HEADS)
    spike_random_key, nesting_random_key = jax.random.split(every_key_row[5])
    spike_amount = jax.random.uniform(spike_random_key, (ROLLOUT_COUNT, ROLLOUT_LENGTH, LOCAL_HEADS)) < 3.0 / ROLLOUT_LENGTH
    nesting_level = jax.random.uniform(nesting_random_key, (ROLLOUT_COUNT, ROLLOUT_LENGTH, LOCAL_HEADS), minval=math.log(0.5), maxval=math.log(0.8))
    return (-decay_speed[None, None, :] * approximate_estimate * machine_multiplier + jnp.where(spike_amount, nesting_level, 0.0)).astype(jnp.float32)


def touch_ends(drawn, rng, least, high):
    extent = drawn.shape
    index_at = [jax.random.randint(jax.random.fold_in(rng, axis), (), 0, extent[axis]) for axis in range(len(extent))]
    drawn = drawn.at[tuple(index_at)].set(least)
    longest = extent.index(max(extent))
    index_at[longest] = (index_at[longest] + 1) % extent[longest]
    return drawn.at[tuple(index_at)].set(high)


def steps_of(key, shape, pieces, least, largest):
    def one(dim, blocks):
        heights = jax.random.uniform(jax.random.fold_in(jax.random.fold_in(key, 6), dim), (blocks,), jnp.float32, least / len(pieces), largest / len(pieces))
        return jnp.repeat(jnp.exp(heights), shape[dim] // blocks).reshape((-1,) + (1,) * (len(shape) - dim - 1))

    loudness = one(*pieces[0])
    for cut in pieces[1:]:
        loudness = loudness * one(*cut)
    return loudness


def noise(own_key, dims, scale, reach, cuts=(), held_as=jnp.bfloat16):
    drawn = jax.random.normal(own_key, dims, jnp.float32) * scale
    if len(cuts) > 0:
        drawn = steps_of(own_key, dims, cuts, -0.22, 0.18) * drawn
    return jnp.clip(drawn, min=-reach, max=reach).astype(held_as)


def setup_inputs(seed: int = 0) -> dict:
    splits = jax.random.split(jax.random.key(seed), 9)
    return {
        "query": noise(splits[0], (ROLLOUT_COUNT, ROLLOUT_LENGTH, LOCAL_HEADS * HD), (ROLLOUT_LENGTH ** -0.25), 0.75, ((0, 4), (1, 8))),
        "keys": noise(splits[1], (ROLLOUT_COUNT, ROLLOUT_LENGTH, LOCAL_HEADS * HD), (ROLLOUT_LENGTH ** -0.25), 0.75, ((0, 4), (1, 8))),
        "values": noise(splits[2], (ROLLOUT_COUNT, ROLLOUT_LENGTH, LOCAL_HEADS * HD), 1.0, 6.0, ((0, 4), (1, 8))),
        "upstream": noise(splits[3], (ROLLOUT_COUNT, ROLLOUT_LENGTH, DM), (ROLLOUT_LENGTH ** -0.25), 0.75, ((0, 4), (1, 8))),
        "out_weight": noise(splits[4], (LOCAL_HEADS * HD, DM), DM ** -0.5, 0.125),
        "log_decay": draw_log_decay(jax.random.fold_in(splits[8], 71), 0),
        "signs": touch_ends((jax.random.randint(splits[6], (ROLLOUT_COUNT, ROLLOUT_LENGTH), 0, 2) < 1).astype(jnp.int32), jax.random.fold_in(splits[6], 1), 0, 1),
        "magnitude": jnp.clip(jnp.exp(math.log(2.0) - 1.3862944 * jax.random.uniform(splits[7], (ROLLOUT_COUNT, ROLLOUT_LENGTH), jnp.float32) ** steps_of(splits[7], (ROLLOUT_COUNT, ROLLOUT_LENGTH), ((0, 4), (1, 8)), -0.2, 0.2)), 0.5, 2.0),
    }


def local_terms(query_heads, key_heads, value_heads, dout_heads, decay_log, scale):
    length_all = query_heads.shape[0]
    blocks = length_all // BLOCK

    def split_blocks(array):
        return array.reshape((blocks, BLOCK) + array.shape[1:])

    inputs_all = tuple(split_blocks(array) for array in (query_heads, key_heads, value_heads, dout_heads, decay_log))
    lower_mask = (jnp.arange(BLOCK)[:, None] >= jnp.arange(BLOCK)[None, :])[None]

    def forward(state, inputs_block):
        query_block, key_block, value_block, dout_block, decay_block = inputs_block
        query_f32 = query_block.astype(jnp.float32)
        key_f32 = key_block.astype(jnp.float32)
        value_f32 = value_block.astype(jnp.float32)
        dout_f32 = dout_block.astype(jnp.float32)
        cumulate = jnp.cumsum(decay_block, axis=0)
        spread = cumulate.T[:, :, None] - cumulate.T[:, None, :]
        weight = jnp.where(lower_mask, jnp.exp(jnp.where(lower_mask, spread, 0.0)), 0.0)
        scores = jnp.einsum("thd,shd->hts", query_f32, key_f32)
        dscores = jnp.einsum("thd,shd->hts", dout_f32, value_f32)
        probs = (scale * scores * weight).astype(jnp.bfloat16).astype(jnp.float32)
        dprobs = (scale * dscores * weight).astype(jnp.bfloat16).astype(jnp.float32)
        attend = jnp.einsum("hts,shd->thd", probs, value_f32)
        grad_q = jnp.einsum("hts,shd->thd", dprobs, key_f32)
        grad_k = jnp.einsum("hts,thd->shd", dprobs, query_f32)
        grad_v = jnp.einsum("hts,thd->shd", probs, dout_f32)
        growth = jnp.exp(cumulate)[:, :, None]
        attend = attend + scale * growth * jnp.einsum("thd,hde->the", query_f32, state, precision=lax.Precision.HIGHEST)
        grad_q = grad_q + scale * growth * jnp.einsum("hde,the->thd", state, dout_f32, precision=lax.Precision.HIGHEST)
        remain = jnp.exp(cumulate[-1][None, :] - cumulate)[:, :, None]
        state = jnp.exp(cumulate[-1])[:, None, None] * state + jnp.einsum("shd,she->hde", key_f32 * remain, value_f32, precision=lax.Precision.HIGHEST)
        return state, (attend, grad_q, grad_k, grad_v)

    def reverse(carry, inputs_block):
        query_block, key_block, value_block, dout_block, decay_block = inputs_block
        query_f32 = query_block.astype(jnp.float32)
        key_f32 = key_block.astype(jnp.float32)
        value_f32 = value_block.astype(jnp.float32)
        dout_f32 = dout_block.astype(jnp.float32)
        cumulate = jnp.cumsum(decay_block, axis=0)
        remain = jnp.exp(cumulate[-1][None, :] - cumulate)[:, :, None]
        growth = jnp.exp(cumulate)[:, :, None]
        grad_k = scale * remain * jnp.einsum("hde,she->shd", carry, value_f32, precision=lax.Precision.HIGHEST)
        grad_v = scale * remain * jnp.einsum("hde,shd->she", carry, key_f32, precision=lax.Precision.HIGHEST)
        carry = jnp.exp(cumulate[-1])[:, None, None] * carry + jnp.einsum("thd,the->hde", query_f32 * growth, dout_f32, precision=lax.Precision.HIGHEST)
        return carry, (grad_k, grad_v)

    start_state = jnp.zeros((query_heads.shape[1], query_heads.shape[2], query_heads.shape[2]), jnp.float32)
    state_end, parts = lax.scan(forward, start_state, inputs_all)
    back_end, back_parts = lax.scan(reverse, start_state, inputs_all, reverse=True)

    def unsplit(array):
        return array.reshape((length_all,) + array.shape[2:])

    return (unsplit(parts[0]), unsplit(parts[1]), unsplit(parts[2] + back_parts[0]),
            unsplit(parts[3] + back_parts[1]), state_end, back_end)


def reference(query, keys, values, upstream, out_weight, log_decay, signs, magnitude):
    scale = HD ** -0.5
    advantage = (2 * signs - 1).astype(jnp.float32) * magnitude
    weighted = (advantage[:, :, None] * upstream.astype(jnp.float32)).astype(jnp.bfloat16)
    flat = weighted.reshape(ROLLOUT_COUNT * ROLLOUT_LENGTH, DM)
    dout = jnp.dot(flat, out_weight.T, preferred_element_type=jnp.float32).astype(jnp.bfloat16)
    dout = dout.reshape(ROLLOUT_COUNT, ROLLOUT_LENGTH, LOCAL_HEADS * HD)

    def one_rollout(inputs_one):
        query_one, key_one, value_one, dout_one, decay_one = inputs_one
        result = local_terms(query_one.reshape(ROLLOUT_LENGTH, LOCAL_HEADS, HD), key_one.reshape(ROLLOUT_LENGTH, LOCAL_HEADS, HD),
                             value_one.reshape(ROLLOUT_LENGTH, LOCAL_HEADS, HD), dout_one.reshape(ROLLOUT_LENGTH, LOCAL_HEADS, HD),
                             decay_one, scale)
        return result[0], result[1], result[2], result[3]

    attend, grad_q, grad_k, grad_v = lax.map(one_rollout, (query, keys, values, dout, log_decay))
    attn = attend.reshape(ROLLOUT_COUNT * ROLLOUT_LENGTH, LOCAL_HEADS * HD).astype(jnp.bfloat16)
    grad_weight = jnp.dot(attn.T, flat, preferred_element_type=jnp.float32)
    shape_out = (ROLLOUT_COUNT, ROLLOUT_LENGTH, LOCAL_HEADS * HD)
    return (grad_q.reshape(shape_out).astype(jnp.bfloat16), grad_k.reshape(shape_out).astype(jnp.bfloat16),
            grad_v.reshape(shape_out).astype(jnp.bfloat16), grad_weight)
```

```python
import jax
import jax.numpy as jnp
from jax import lax
from jax.sharding import PartitionSpec as P

LOCAL_HEADS = 16
HD = 128
BLOCK = 512


def carried_in(value, axis, join, backward):
    count = lax.axis_size(axis)
    step = -1 if backward else 1
    partial = value
    gathered = None
    distance = 1
    while distance < count:
        pairs = [(i, i + step * distance) for i in range(count) if 0 <= i + step * distance < count]
        arrived = jax.tree.map(lambda part: lax.ppermute(part, axis, pairs), partial)
        gathered = arrived if gathered is None else join(arrived, gathered)
        if distance * 2 < count:
            partial = join(arrived, partial)
        distance *= 2
    if gathered is None:
        gathered = jax.tree.map(jnp.zeros_like, value)
    return gathered


def block_terms(query_block, key_block, value_block, dout_block, decay_block, scale, lower_mask):
    cumulate = jnp.cumsum(decay_block, axis=0)
    spread = cumulate.T[:, :, None] - cumulate.T[:, None, :]
    weight = jnp.where(lower_mask, jnp.exp(jnp.where(lower_mask, spread, 0.0)), 0.0)
    scores = jnp.einsum("thd,shd->hts", query_block, key_block, preferred_element_type=jnp.float32)
    dscores = jnp.einsum(
        "thd,shd->hts", dout_block, value_block, preferred_element_type=jnp.float32
    )
    probs = (scale * scores * weight).astype(jnp.bfloat16)
    dprobs = (scale * dscores * weight).astype(jnp.bfloat16)
    attend = jnp.einsum("hts,shd->thd", probs, value_block, preferred_element_type=jnp.float32)
    grad_q = jnp.einsum("hts,shd->thd", dprobs, key_block, preferred_element_type=jnp.float32)
    grad_k = jnp.einsum("hts,thd->shd", dprobs, query_block, preferred_element_type=jnp.float32)
    grad_v = jnp.einsum("hts,thd->shd", probs, dout_block, preferred_element_type=jnp.float32)
    growth = jnp.exp(cumulate)[:, :, None]
    remain = jnp.exp(cumulate[-1][None, :] - cumulate)[:, :, None]
    state_own = jnp.einsum(
        "shd,she->hde",
        key_block.astype(jnp.float32) * remain,
        value_block.astype(jnp.float32),
        precision=lax.Precision.HIGHEST,
    )
    back_own = jnp.einsum(
        "thd,the->hde",
        query_block.astype(jnp.float32) * growth,
        dout_block.astype(jnp.float32),
        precision=lax.Precision.HIGHEST,
    )
    return (attend, grad_q, grad_k, grad_v, state_own, back_own, cumulate[-1])


def local_terms(query_heads, key_heads, value_heads, dout_heads, decay_log, scale):
    lower_mask = (jnp.arange(BLOCK)[:, None] >= jnp.arange(BLOCK)[None, :])[None]
    attend, grad_q, grad_k, grad_v, state_end, back_end, last_total = block_terms(
        query_heads, key_heads, value_heads, dout_heads, decay_log, scale, lower_mask
    )
    return (attend, grad_q, grad_k, grad_v, state_end, back_end)


def chain_join(earlier, later):
    return (earlier[0] + later[0], jnp.exp(later[0])[:, None, None] * earlier[1] + later[1])


def on_device(query, keys, values, upstream, out_weight, log_decay, signs, magnitude):
    tokens = query.shape[1]
    width = query.shape[2]
    scale = HD ** (-0.5)
    advantage = (2 * signs[0] - 1).astype(jnp.float32) * magnitude[0]
    weighted = (advantage[:, None] * upstream[0].astype(jnp.float32)).astype(jnp.bfloat16)
    dout = lax.dot_general(
        weighted, out_weight, (((1,), (1,)), ((), ())), preferred_element_type=jnp.float32
    ).astype(jnp.bfloat16)

    def to_heads(array):
        return array.reshape(tokens, LOCAL_HEADS, HD)

    decay_here = log_decay[0]
    query_heads = to_heads(query[0])
    key_heads = to_heads(keys[0])
    value_heads = to_heads(values[0])
    dout_heads = to_heads(dout)
    attend, grad_q, grad_k, grad_v, state_end, back_end = local_terms(
        query_heads, key_heads, value_heads, dout_heads, decay_here, scale
    )
    running = jnp.cumsum(decay_here, axis=0)
    total = running[-1]
    state_in = carried_in((total, state_end), "ctx", chain_join, False)[1]
    back_in = carried_in((total, back_end), "ctx", chain_join, True)[1]
    query_f32 = query_heads.astype(jnp.float32)
    key_f32 = key_heads.astype(jnp.float32)
    value_f32 = value_heads.astype(jnp.float32)
    dout_f32 = dout_heads.astype(jnp.float32)
    growth = jnp.exp(running)[:, :, None]
    remain = jnp.exp(total[None, :] - running)[:, :, None]
    attend = attend + scale * growth * jnp.einsum(
        "thd,hde->the", query_f32, state_in, precision=lax.Precision.HIGHEST
    )
    grad_q = grad_q + scale * growth * jnp.einsum(
        "hde,the->thd", state_in, dout_f32, precision=lax.Precision.HIGHEST
    )
    grad_k = grad_k + scale * remain * jnp.einsum(
        "hde,she->shd", back_in, value_f32, precision=lax.Precision.HIGHEST
    )
    grad_v = grad_v + scale * remain * jnp.einsum(
        "hde,shd->she", back_in, key_f32, precision=lax.Precision.HIGHEST
    )
    attn = attend.reshape(tokens, width).astype(jnp.bfloat16)
    grad_weight = lax.psum_scatter(
        lax.dot_general(
            attn, weighted, (((0,), (0,)), ((), ())), preferred_element_type=jnp.float32
        ),
        ("ctx", "dp"),
        scatter_dimension=0,
        tiled=True,
    )
    shape_out = (1, tokens, width)
    return (
        grad_q.reshape(shape_out).astype(jnp.bfloat16),
        grad_k.reshape(shape_out).astype(jnp.bfloat16),
        grad_v.reshape(shape_out).astype(jnp.bfloat16),
        grad_weight,
    )


def solution(mesh):
    in_specs = (
        P("dp", "ctx", None),
        P("dp", "ctx", None),
        P("dp", "ctx", None),
        P("dp", "ctx", None),
        P(),
        P("dp", "ctx", None),
        P("dp", "ctx"),
        P("dp", "ctx"),
    )
    out_specs = (
        P("dp", "ctx", None),
        P("dp", "ctx", None),
        P("dp", "ctx", None),
        P(("ctx", "dp"), None),
    )
    return jax.shard_map(
        on_device, mesh=mesh, in_specs=in_specs, out_specs=out_specs, check_vma=False
    )
```

```python
import jax
import jax.numpy as jnp
from jax import lax
from jax.sharding import PartitionSpec as P

LOCAL_HEADS = 16
HD = 128
BLOCK = 512


def carried_in(value, axis, join, backward):
    count = lax.axis_size(axis)
    step = -1 if backward else 1
    partial = value
    gathered = None
    distance = 1
    while distance < count:
        pairs = [(i, i + step * distance) for i in range(count) if 0 <= i + step * distance < count]
        arrived = jax.tree.map(lambda part: lax.ppermute(part, axis, pairs), partial)
        gathered = arrived if gathered is None else join(arrived, gathered)
        if distance * 2 < count:
            partial = join(arrived, partial)
        distance *= 2
    if gathered is None:
        gathered = jax.tree.map(jnp.zeros_like, value)
    return gathered


def decay_weights(cumulate, lower_mask):
    spread = cumulate.T[:, :, None] - cumulate.T[:, None, :]
    return jnp.where(lower_mask, jnp.exp(jnp.where(lower_mask, spread, 0.0)), 0.0)


def chain_join(earlier, later):
    return (earlier[0] + later[0], jnp.exp(later[0])[:, None, None] * earlier[1] + later[1])


def on_device(query, keys, values, upstream, out_weight, log_decay, signs, magnitude):
    tokens = query.shape[1]
    width = query.shape[2]
    scale = HD ** (-0.5)

    def to_heads(array):
        return array.reshape(tokens, LOCAL_HEADS, HD)

    decay_here = log_decay[0]
    running = jnp.cumsum(decay_here, axis=0)
    total = running[-1]
    growth = jnp.exp(running)[:, :, None]
    remain = jnp.exp(total[None, :] - running)[:, :, None]
    query_heads = to_heads(query[0])
    key_heads = to_heads(keys[0])
    value_heads = to_heads(values[0])
    query_f32 = query_heads.astype(jnp.float32)
    key_f32 = key_heads.astype(jnp.float32)
    value_f32 = value_heads.astype(jnp.float32)

    state_end = jnp.einsum(
        "shd,she->hde", key_f32 * remain, value_f32, precision=lax.Precision.HIGHEST
    )
    state_in = carried_in((total, state_end), "ctx", chain_join, False)[1]

    advantage = (2 * signs[0] - 1).astype(jnp.float32) * magnitude[0]
    weighted = (advantage[:, None] * upstream[0].astype(jnp.float32)).astype(jnp.bfloat16)
    dout = lax.dot_general(
        weighted, out_weight, (((1,), (1,)), ((), ())), preferred_element_type=jnp.float32
    ).astype(jnp.bfloat16)
    dout_heads = to_heads(dout)
    dout_f32 = dout_heads.astype(jnp.float32)
    back_end = jnp.einsum(
        "thd,the->hde", query_f32 * growth, dout_f32, precision=lax.Precision.HIGHEST
    )
    back_in = carried_in((total, back_end), "ctx", chain_join, True)[1]

    lower_mask = (jnp.arange(BLOCK)[:, None] >= jnp.arange(BLOCK)[None, :])[None]
    weight = decay_weights(running, lower_mask)
    scores = jnp.einsum("thd,shd->hts", query_heads, key_heads, preferred_element_type=jnp.float32)
    probs = (scale * scores * weight).astype(jnp.bfloat16)
    attend = jnp.einsum("hts,shd->thd", probs, value_heads, preferred_element_type=jnp.float32)
    attend = attend + scale * growth * jnp.einsum(
        "thd,hde->the", query_f32, state_in, precision=lax.Precision.HIGHEST
    )
    attn = attend.reshape(tokens, width).astype(jnp.bfloat16)
    partial = lax.dot_general(
        attn, weighted, (((0,), (0,)), ((), ())), preferred_element_type=jnp.float32
    )
    (partial, back_in, state_in, probs, weight, query_heads, key_heads, value_heads,
     dout_heads) = lax.optimization_barrier(
        (partial, back_in, state_in, probs, weight, query_heads, key_heads, value_heads,
         dout_heads))
    grad_weight = lax.psum_scatter(partial, ("ctx", "dp"), scatter_dimension=0, tiled=True)

    query_f32 = query_heads.astype(jnp.float32)
    key_f32 = key_heads.astype(jnp.float32)
    value_f32 = value_heads.astype(jnp.float32)
    dout_f32 = dout_heads.astype(jnp.float32)
    dscores = jnp.einsum(
        "thd,shd->hts", dout_heads, value_heads, preferred_element_type=jnp.float32
    )
    dprobs = (scale * dscores * weight).astype(jnp.bfloat16)
    grad_q = jnp.einsum("hts,shd->thd", dprobs, key_heads, preferred_element_type=jnp.float32)
    grad_k = jnp.einsum("hts,thd->shd", dprobs, query_heads, preferred_element_type=jnp.float32)
    grad_v = jnp.einsum("hts,thd->shd", probs, dout_heads, preferred_element_type=jnp.float32)
    grad_q = grad_q + scale * growth * jnp.einsum(
        "hde,the->thd", state_in, dout_f32, precision=lax.Precision.HIGHEST
    )
    grad_k = grad_k + scale * remain * jnp.einsum(
        "hde,she->shd", back_in, value_f32, precision=lax.Precision.HIGHEST
    )
    grad_v = grad_v + scale * remain * jnp.einsum(
        "hde,shd->she", back_in, key_f32, precision=lax.Precision.HIGHEST
    )
    shape_out = (1, tokens, width)
    return (
        grad_q.reshape(shape_out).astype(jnp.bfloat16),
        grad_k.reshape(shape_out).astype(jnp.bfloat16),
        grad_v.reshape(shape_out).astype(jnp.bfloat16),
        grad_weight,
    )


def solution(mesh):
    in_specs = (
        P("dp", "ctx", None),
        P("dp", "ctx", None),
        P("dp", "ctx", None),
        P("dp", "ctx", None),
        P(),
        P("dp", "ctx", None),
        P("dp", "ctx"),
        P("dp", "ctx"),
    )
    out_specs = (
        P("dp", "ctx", None),
        P("dp", "ctx", None),
        P("dp", "ctx", None),
        P(("ctx", "dp"), None),
    )
    return jax.shard_map(
        on_device, mesh=mesh, in_specs=in_specs, out_specs=out_specs, check_vma=False
    )
```

```python
import jax
import jax.numpy as jnp
from jax import lax
from jax.sharding import PartitionSpec as P

LOCAL_HEADS = 16
HD = 128
BLOCK = 512


def carried_in(value, axis, join, backward):
    count = lax.axis_size(axis)
    step = -1 if backward else 1
    partial = value
    gathered = None
    distance = 1
    while distance < count:
        pairs = [(i, i + step * distance) for i in range(count) if 0 <= i + step * distance < count]
        arrived = jax.tree.map(lambda part: lax.ppermute(part, axis, pairs), partial)
        gathered = arrived if gathered is None else join(arrived, gathered)
        if distance * 2 < count:
            partial = join(arrived, partial)
        distance *= 2
    if gathered is None:
        gathered = jax.tree.map(jnp.zeros_like, value)
    return gathered


def decay_weights(cumulate, lower_mask):
    spread = cumulate.T[:, :, None] - cumulate.T[:, None, :]
    return jnp.where(lower_mask, jnp.exp(jnp.where(lower_mask, spread, 0.0)), 0.0)


def chain_join(earlier, later):
    return (earlier[0] + later[0], jnp.exp(later[0])[:, None, None] * earlier[1] + later[1])


def on_device(query, keys, values, upstream, out_weight, log_decay, signs, magnitude):
    tokens = query.shape[1]
    width = query.shape[2]
    scale = HD ** (-0.5)

    def to_heads(array):
        return array.reshape(tokens, LOCAL_HEADS, HD)

    decay_here = log_decay[0]
    running = jnp.cumsum(decay_here, axis=0)
    total = running[-1]
    growth = jnp.exp(running)[:, :, None]
    remain = jnp.exp(total[None, :] - running)[:, :, None]
    query_heads = to_heads(query[0])
    key_heads = to_heads(keys[0])
    value_heads = to_heads(values[0])
    query_f32 = query_heads.astype(jnp.float32)
    key_f32 = key_heads.astype(jnp.float32)
    value_f32 = value_heads.astype(jnp.float32)

    state_end = jnp.einsum(
        "shd,she->hde", key_f32 * remain, value_f32, precision=lax.Precision.HIGHEST
    )
    state_in = carried_in((total, state_end), "ctx", chain_join, False)[1]
    state_end, upstream, query_heads = lax.optimization_barrier((state_end, upstream, query_heads))

    advantage = (2 * signs[0] - 1).astype(jnp.float32) * magnitude[0]
    weighted = (advantage[:, None] * upstream[0].astype(jnp.float32)).astype(jnp.bfloat16)
    dout = lax.dot_general(
        weighted, out_weight, (((1,), (1,)), ((), ())), preferred_element_type=jnp.float32
    ).astype(jnp.bfloat16)
    dout_heads = to_heads(dout)
    dout_f32 = dout_heads.astype(jnp.float32)
    back_end = jnp.einsum(
        "thd,the->hde", query_f32 * growth, dout_f32, precision=lax.Precision.HIGHEST
    )

    lower_mask = (jnp.arange(BLOCK)[:, None] >= jnp.arange(BLOCK)[None, :])[None]
    weight = decay_weights(running, lower_mask)
    scores = jnp.einsum("thd,shd->hts", query_heads, key_heads, preferred_element_type=jnp.float32)
    probs = (scale * scores * weight).astype(jnp.bfloat16)
    attend = jnp.einsum("hts,shd->thd", probs, value_heads, preferred_element_type=jnp.float32)
    attend = attend + scale * growth * jnp.einsum(
        "thd,hde->the", query_f32, state_in, precision=lax.Precision.HIGHEST
    )
    attn = attend.reshape(tokens, width).astype(jnp.bfloat16)
    partial = lax.dot_general(
        attn, weighted, (((0,), (0,)), ((), ())), preferred_element_type=jnp.float32
    )
    partial, back_end = lax.optimization_barrier((partial, back_end))
    grad_weight = lax.psum_scatter(partial, ("ctx", "dp"), scatter_dimension=0, tiled=True)
    back_in = carried_in((total, back_end), "ctx", chain_join, True)[1]

    dscores = jnp.einsum(
        "thd,shd->hts", dout_heads, value_heads, preferred_element_type=jnp.float32
    )
    dprobs = (scale * dscores * weight).astype(jnp.bfloat16)
    grad_q = jnp.einsum("hts,shd->thd", dprobs, key_heads, preferred_element_type=jnp.float32)
    grad_k = jnp.einsum("hts,thd->shd", dprobs, query_heads, preferred_element_type=jnp.float32)
    grad_v = jnp.einsum("hts,thd->shd", probs, dout_heads, preferred_element_type=jnp.float32)
    grad_q = grad_q + scale * growth * jnp.einsum(
        "hde,the->thd", state_in, dout_f32, precision=lax.Precision.HIGHEST
    )
    grad_k = grad_k + scale * remain * jnp.einsum(
        "hde,she->shd", back_in, value_f32, precision=lax.Precision.HIGHEST
    )
    grad_v = grad_v + scale * remain * jnp.einsum(
        "hde,shd->she", back_in, key_f32, precision=lax.Precision.HIGHEST
    )
    shape_out = (1, tokens, width)
    return (
        grad_q.reshape(shape_out).astype(jnp.bfloat16),
        grad_k.reshape(shape_out).astype(jnp.bfloat16),
        grad_v.reshape(shape_out).astype(jnp.bfloat16),
        grad_weight,
    )


def solution(mesh):
    in_specs = (
        P("dp", "ctx", None),
        P("dp", "ctx", None),
        P("dp", "ctx", None),
        P("dp", "ctx", None),
        P(),
        P("dp", "ctx", None),
        P("dp", "ctx"),
        P("dp", "ctx"),
    )
    out_specs = (
        P("dp", "ctx", None),
        P("dp", "ctx", None),
        P("dp", "ctx", None),
        P(("ctx", "dp"), None),
    )
    return jax.shard_map(
        on_device, mesh=mesh, in_specs=in_specs, out_specs=out_specs, check_vma=False
    )
```

```python
import jax
import jax.numpy as jnp
from jax import lax
from jax.sharding import PartitionSpec as P

LOCAL_HEADS = 16
HD = 128
BLOCK = 512


def carried_in(value, join, even_backward):
    count, groups = lax.axis_size("ctx"), lax.axis_size("dp")
    partial = value
    gathered = None
    distance = 1
    while distance < count:
        pairs = []
        for place in range(count):
            for group in range(groups):
                step = -distance if (group % 2 == 0) == even_backward else distance
                if 0 <= place + step < count:
                    pairs.append((place * groups + group, (place + step) * groups + group))
        arrived = jax.tree.map(lambda part: lax.ppermute(part, ("ctx", "dp"), pairs), partial)
        gathered = arrived if gathered is None else join(arrived, gathered)
        if distance * 2 < count:
            partial = join(arrived, partial)
        distance *= 2
    if gathered is None:
        gathered = jax.tree.map(jnp.zeros_like, value)
    return gathered


def decay_weights(cumulate, lower_mask):
    spread = cumulate.T[:, :, None] - cumulate.T[:, None, :]
    return jnp.where(lower_mask, jnp.exp(jnp.where(lower_mask, spread, 0.0)), 0.0)


def chain_join(earlier, later):
    return (earlier[0] + later[0], jnp.exp(later[0])[:, None, None] * earlier[1] + later[1])


def on_device(query, keys, values, upstream, out_weight, log_decay, signs, magnitude):
    tokens = query.shape[1]
    width = query.shape[2]
    scale = HD ** (-0.5)

    def to_heads(array):
        return array.reshape(tokens, LOCAL_HEADS, HD)

    decay_here = log_decay[0]
    running = jnp.cumsum(decay_here, axis=0)
    total = running[-1]
    growth = jnp.exp(running)[:, :, None]
    remain = jnp.exp(total[None, :] - running)[:, :, None]
    query_heads = to_heads(query[0])
    key_heads = to_heads(keys[0])
    value_heads = to_heads(values[0])
    query_f32 = query_heads.astype(jnp.float32)
    key_f32 = key_heads.astype(jnp.float32)
    value_f32 = value_heads.astype(jnp.float32)

    state_end = jnp.einsum(
        "shd,she->hde", key_f32 * remain, value_f32, precision=lax.Precision.HIGHEST
    )

    advantage = (2 * signs[0] - 1).astype(jnp.float32) * magnitude[0]
    weighted = (advantage[:, None] * upstream[0].astype(jnp.float32)).astype(jnp.bfloat16)
    dout = lax.dot_general(
        weighted, out_weight, (((1,), (1,)), ((), ())), preferred_element_type=jnp.float32
    ).astype(jnp.bfloat16)
    dout_heads = to_heads(dout)
    dout_f32 = dout_heads.astype(jnp.float32)
    back_end = jnp.einsum(
        "thd,the->hde", query_f32 * growth, dout_f32, precision=lax.Precision.HIGHEST
    )
    even = lax.axis_index("dp") % 2 == 0
    first = carried_in((total, jnp.where(even, state_end, back_end)), chain_join, False)[1]
    second_end, first = lax.optimization_barrier((jnp.where(even, back_end, state_end), first))
    second = carried_in((total, second_end), chain_join, True)[1]
    state_in = jnp.where(even, first, second)
    back_in = jnp.where(even, second, first)

    lower_mask = (jnp.arange(BLOCK)[:, None] >= jnp.arange(BLOCK)[None, :])[None]
    weight = decay_weights(running, lower_mask)
    scores = jnp.einsum("thd,shd->hts", query_heads, key_heads, preferred_element_type=jnp.float32)
    probs = (scale * scores * weight).astype(jnp.bfloat16)
    attend = jnp.einsum("hts,shd->thd", probs, value_heads, preferred_element_type=jnp.float32)
    attend = attend + scale * growth * jnp.einsum(
        "thd,hde->the", query_f32, state_in, precision=lax.Precision.HIGHEST
    )
    attn = attend.reshape(tokens, width).astype(jnp.bfloat16)
    partial = lax.dot_general(
        attn, weighted, (((0,), (0,)), ((), ())), preferred_element_type=jnp.float32
    )
    partial, back_in = lax.optimization_barrier((partial, back_in))
    grad_weight = lax.psum_scatter(partial, ("ctx", "dp"), scatter_dimension=0, tiled=True)

    dscores = jnp.einsum(
        "thd,shd->hts", dout_heads, value_heads, preferred_element_type=jnp.float32
    )
    dprobs = (scale * dscores * weight).astype(jnp.bfloat16)
    grad_q = jnp.einsum("hts,shd->thd", dprobs, key_heads, preferred_element_type=jnp.float32)
    grad_k = jnp.einsum("hts,thd->shd", dprobs, query_heads, preferred_element_type=jnp.float32)
    grad_v = jnp.einsum("hts,thd->shd", probs, dout_heads, preferred_element_type=jnp.float32)
    grad_q = grad_q + scale * growth * jnp.einsum(
        "hde,the->thd", state_in, dout_f32, precision=lax.Precision.HIGHEST
    )
    grad_k = grad_k + scale * remain * jnp.einsum(
        "hde,she->shd", back_in, value_f32, precision=lax.Precision.HIGHEST
    )
    grad_v = grad_v + scale * remain * jnp.einsum(
        "hde,shd->she", back_in, key_f32, precision=lax.Precision.HIGHEST
    )
    shape_out = (1, tokens, width)
    return (
        grad_q.reshape(shape_out).astype(jnp.bfloat16),
        grad_k.reshape(shape_out).astype(jnp.bfloat16),
        grad_v.reshape(shape_out).astype(jnp.bfloat16),
        grad_weight,
    )


def solution(mesh):
    in_specs = (
        P("dp", "ctx", None),
        P("dp", "ctx", None),
        P("dp", "ctx", None),
        P("dp", "ctx", None),
        P(),
        P("dp", "ctx", None),
        P("dp", "ctx"),
        P("dp", "ctx"),
    )
    out_specs = (
        P("dp", "ctx", None),
        P("dp", "ctx", None),
        P("dp", "ctx", None),
        P(("ctx", "dp"), None),
    )
    return jax.shard_map(
        on_device, mesh=mesh, in_specs=in_specs, out_specs=out_specs, check_vma=False
    )
```

```python
import jax
import jax.numpy as jnp
from jax import lax
from jax.sharding import PartitionSpec as P

LOCAL_HEADS = 16
HD = 128
BLOCK = 512


def carried_in(value, axis, join, backward):
    count = lax.axis_size(axis)
    step = -1 if backward else 1
    partial = value
    gathered = None
    distance = 1
    while distance < count:
        pairs = [(i, i + step * distance) for i in range(count) if 0 <= i + step * distance < count]
        arrived = jax.tree.map(lambda part: lax.ppermute(part, axis, pairs), partial)
        gathered = arrived if gathered is None else join(arrived, gathered)
        if distance * 2 < count:
            partial = join(arrived, partial)
        distance *= 2
    if gathered is None:
        gathered = jax.tree.map(jnp.zeros_like, value)
    return gathered


def decay_weights(cumulate, lower_mask):
    spread = cumulate.T[:, :, None] - cumulate.T[:, None, :]
    return jnp.where(lower_mask, jnp.exp(jnp.where(lower_mask, spread, 0.0)), 0.0)


def chain_join(earlier, later):
    return (earlier[0] + later[0], jnp.exp(later[0])[:, None, None] * earlier[1] + later[1])


def pack_state(total, state):
    slab = jnp.broadcast_to(total[:, None, None], (state.shape[0], 8, state.shape[2]))
    return jnp.concatenate([state, slab], axis=1)


def packed_join(earlier, later):
    rows = earlier.shape[1] - 8
    joined = chain_join((earlier[:, rows, 0], earlier[:, :rows]), (later[:, rows, 0], later[:, :rows]))
    return pack_state(*joined)


def on_device(query, keys, values, upstream, out_weight, log_decay, signs, magnitude):
    tokens = query.shape[1]
    width = query.shape[2]
    scale = HD ** (-0.5)

    def to_heads(array):
        return array.reshape(tokens, LOCAL_HEADS, HD)

    decay_here = log_decay[0]
    running = jnp.cumsum(decay_here, axis=0)
    total = running[-1]
    growth = jnp.exp(running)[:, :, None]
    remain = jnp.exp(total[None, :] - running)[:, :, None]
    query_heads = to_heads(query[0])
    key_heads = to_heads(keys[0])
    value_heads = to_heads(values[0])
    query_f32 = query_heads.astype(jnp.float32)
    key_f32 = key_heads.astype(jnp.float32)
    value_f32 = value_heads.astype(jnp.float32)

    state_end = jnp.einsum(
        "shd,she->hde", key_f32 * remain, value_f32, precision=lax.Precision.HIGHEST
    )
    state_in = carried_in(pack_state(total, state_end), "ctx", packed_join, False)[:, :HD]
    state_end, upstream, query_heads = lax.optimization_barrier((state_end, upstream, query_heads))

    advantage = (2 * signs[0] - 1).astype(jnp.float32) * magnitude[0]
    weighted = (advantage[:, None] * upstream[0].astype(jnp.float32)).astype(jnp.bfloat16)
    dout = lax.dot_general(
        weighted, out_weight, (((1,), (1,)), ((), ())), preferred_element_type=jnp.float32
    ).astype(jnp.bfloat16)
    dout_heads = to_heads(dout)
    dout_f32 = dout_heads.astype(jnp.float32)
    back_end = jnp.einsum(
        "thd,the->hde", query_f32 * growth, dout_f32, precision=lax.Precision.HIGHEST
    )

    lower_mask = (jnp.arange(BLOCK)[:, None] >= jnp.arange(BLOCK)[None, :])[None]
    weight = decay_weights(running, lower_mask)
    scores = jnp.einsum("thd,shd->hts", query_heads, key_heads, preferred_element_type=jnp.float32)
    probs = (scale * scores * weight).astype(jnp.bfloat16)
    attend = jnp.einsum("hts,shd->thd", probs, value_heads, preferred_element_type=jnp.float32)
    attend = attend + scale * growth * jnp.einsum(
        "thd,hde->the", query_f32, state_in, precision=lax.Precision.HIGHEST
    )
    attn = attend.reshape(tokens, width).astype(jnp.bfloat16)
    partial = lax.dot_general(
        attn, weighted, (((0,), (0,)), ((), ())), preferred_element_type=jnp.float32
    )
    partial, back_end = lax.optimization_barrier((partial, back_end))
    grad_weight = lax.psum_scatter(partial, ("ctx", "dp"), scatter_dimension=0, tiled=True)
    back_in = carried_in(pack_state(total, back_end), "ctx", packed_join, True)[:, :HD]

    dscores = jnp.einsum(
        "thd,shd->hts", dout_heads, value_heads, preferred_element_type=jnp.float32
    )
    dprobs = (scale * dscores * weight).astype(jnp.bfloat16)
    grad_q = jnp.einsum("hts,shd->thd", dprobs, key_heads, preferred_element_type=jnp.float32)
    grad_k = jnp.einsum("hts,thd->shd", dprobs, query_heads, preferred_element_type=jnp.float32)
    grad_v = jnp.einsum("hts,thd->shd", probs, dout_heads, preferred_element_type=jnp.float32)
    grad_q = grad_q + scale * growth * jnp.einsum(
        "hde,the->thd", state_in, dout_f32, precision=lax.Precision.HIGHEST
    )
    grad_k = grad_k + scale * remain * jnp.einsum(
        "hde,she->shd", back_in, value_f32, precision=lax.Precision.HIGHEST
    )
    grad_v = grad_v + scale * remain * jnp.einsum(
        "hde,shd->she", back_in, key_f32, precision=lax.Precision.HIGHEST
    )
    shape_out = (1, tokens, width)
    return (
        grad_q.reshape(shape_out).astype(jnp.bfloat16),
        grad_k.reshape(shape_out).astype(jnp.bfloat16),
        grad_v.reshape(shape_out).astype(jnp.bfloat16),
        grad_weight,
    )


def solution(mesh):
    in_specs = (
        P("dp", "ctx", None),
        P("dp", "ctx", None),
        P("dp", "ctx", None),
        P("dp", "ctx", None),
        P(),
        P("dp", "ctx", None),
        P("dp", "ctx"),
        P("dp", "ctx"),
    )
    out_specs = (
        P("dp", "ctx", None),
        P("dp", "ctx", None),
        P("dp", "ctx", None),
        P(("ctx", "dp"), None),
    )
    return jax.shard_map(
        on_device, mesh=mesh, in_specs=in_specs, out_specs=out_specs, check_vma=False
    )
```

```python
import jax
import jax.numpy as jnp
from jax import lax
from jax.sharding import PartitionSpec as P

LOCAL_HEADS = 16
HD = 128
BLOCK = 512


def carried_in(value, axis, join, backward, radix):
    count = lax.axis_size(axis)
    sign = -1 if backward else 1
    partial = value
    gathered = None
    unit = 1
    while unit < count:
        arrivals = []
        for multiple in range(1, radix):
            distance = sign * multiple * unit
            if multiple * unit >= count:
                break
            pairs = [(i, i + distance) for i in range(count) if 0 <= i + distance < count]
            arrivals.append(lax.ppermute(partial, axis, pairs))
        arrived = arrivals[-1]
        for nearer in reversed(arrivals[:-1]):
            arrived = join(arrived, nearer)
        gathered = arrived if gathered is None else join(arrived, gathered)
        if unit * radix < count:
            partial = join(arrived, partial)
        unit *= radix
    if gathered is None:
        gathered = jnp.zeros_like(value)
    return gathered


def decay_weights(cumulate, lower_mask):
    spread = cumulate.T[:, :, None] - cumulate.T[:, None, :]
    return jnp.where(lower_mask, jnp.exp(jnp.where(lower_mask, spread, 0.0)), 0.0)


def chain_join(earlier, later):
    return (earlier[0] + later[0], jnp.exp(later[0])[:, None, None] * earlier[1] + later[1])


def pack_state(total, state):
    slab = jnp.broadcast_to(total[:, None, None], (state.shape[0], 8, state.shape[2]))
    return jnp.concatenate([state, slab], axis=1)


def packed_join(earlier, later):
    rows = earlier.shape[1] - 8
    joined = chain_join((earlier[:, rows, 0], earlier[:, :rows]), (later[:, rows, 0], later[:, :rows]))
    return pack_state(*joined)


def on_device(query, keys, values, upstream, out_weight, log_decay, signs, magnitude):
    tokens = query.shape[1]
    width = query.shape[2]
    scale = HD ** (-0.5)

    def to_heads(array):
        return array.reshape(tokens, LOCAL_HEADS, HD)

    decay_here = log_decay[0]
    running = jnp.cumsum(decay_here, axis=0)
    total = running[-1]
    growth = jnp.exp(running)[:, :, None]
    remain = jnp.exp(total[None, :] - running)[:, :, None]
    query_heads = to_heads(query[0])
    key_heads = to_heads(keys[0])
    value_heads = to_heads(values[0])
    query_f32 = query_heads.astype(jnp.float32)
    key_f32 = key_heads.astype(jnp.float32)
    value_f32 = value_heads.astype(jnp.float32)

    state_end = jnp.einsum(
        "shd,she->hde", key_f32 * remain, value_f32, precision=lax.Precision.HIGHEST
    )
    state_in = carried_in(pack_state(total, state_end), "ctx", packed_join, False, 4)[:, :HD]
    state_end, upstream, query_heads = lax.optimization_barrier((state_end, upstream, query_heads))

    advantage = (2 * signs[0] - 1).astype(jnp.float32) * magnitude[0]
    weighted = (advantage[:, None] * upstream[0].astype(jnp.float32)).astype(jnp.bfloat16)
    dout = lax.dot_general(
        weighted, out_weight, (((1,), (1,)), ((), ())), preferred_element_type=jnp.float32
    ).astype(jnp.bfloat16)
    dout_heads = to_heads(dout)
    dout_f32 = dout_heads.astype(jnp.float32)
    back_end = jnp.einsum(
        "thd,the->hde", query_f32 * growth, dout_f32, precision=lax.Precision.HIGHEST
    )

    lower_mask = (jnp.arange(BLOCK)[:, None] >= jnp.arange(BLOCK)[None, :])[None]
    weight = decay_weights(running, lower_mask)
    scores = jnp.einsum("thd,shd->hts", query_heads, key_heads, preferred_element_type=jnp.float32)
    probs = (scale * scores * weight).astype(jnp.bfloat16)
    attend = jnp.einsum("hts,shd->thd", probs, value_heads, preferred_element_type=jnp.float32)
    attend = attend + scale * growth * jnp.einsum(
        "thd,hde->the", query_f32, state_in, precision=lax.Precision.HIGHEST
    )
    attn = attend.reshape(tokens, width).astype(jnp.bfloat16)
    partial = lax.dot_general(
        attn, weighted, (((0,), (0,)), ((), ())), preferred_element_type=jnp.float32
    )
    partial, back_end = lax.optimization_barrier((partial, back_end))
    grad_weight = lax.psum_scatter(partial, ("ctx", "dp"), scatter_dimension=0, tiled=True)
    back_in = carried_in(pack_state(total, back_end), "ctx", packed_join, True, 2)[:, :HD]

    dscores = jnp.einsum(
        "thd,shd->hts", dout_heads, value_heads, preferred_element_type=jnp.float32
    )
    dprobs = (scale * dscores * weight).astype(jnp.bfloat16)
    grad_q = jnp.einsum("hts,shd->thd", dprobs, key_heads, preferred_element_type=jnp.float32)
    grad_k = jnp.einsum("hts,thd->shd", dprobs, query_heads, preferred_element_type=jnp.float32)
    grad_v = jnp.einsum("hts,thd->shd", probs, dout_heads, preferred_element_type=jnp.float32)
    grad_q = grad_q + scale * growth * jnp.einsum(
        "hde,the->thd", state_in, dout_f32, precision=lax.Precision.HIGHEST
    )
    grad_k = grad_k + scale * remain * jnp.einsum(
        "hde,she->shd", back_in, value_f32, precision=lax.Precision.HIGHEST
    )
    grad_v = grad_v + scale * remain * jnp.einsum(
        "hde,shd->she", back_in, key_f32, precision=lax.Precision.HIGHEST
    )
    shape_out = (1, tokens, width)
    return (
        grad_q.reshape(shape_out).astype(jnp.bfloat16),
        grad_k.reshape(shape_out).astype(jnp.bfloat16),
        grad_v.reshape(shape_out).astype(jnp.bfloat16),
        grad_weight,
    )


def solution(mesh):
    in_specs = (
        P("dp", "ctx", None),
        P("dp", "ctx", None),
        P("dp", "ctx", None),
        P("dp", "ctx", None),
        P(),
        P("dp", "ctx", None),
        P("dp", "ctx"),
        P("dp", "ctx"),
    )
    out_specs = (
        P("dp", "ctx", None),
        P("dp", "ctx", None),
        P("dp", "ctx", None),
        P(("ctx", "dp"), None),
    )
    return jax.shard_map(
        on_device, mesh=mesh, in_specs=in_specs, out_specs=out_specs, check_vma=False
    )
```

```python
import jax
import jax.numpy as jnp
from jax import lax
from jax.sharding import PartitionSpec as P

LOCAL_HEADS = 16
HD = 128
BLOCK = 512


def carried_in(value, axis, join, backward):
    count = lax.axis_size(axis)
    step = -1 if backward else 1
    partial = value
    gathered = None
    distance = 1
    while distance < count:
        pairs = [(i, i + step * distance) for i in range(count) if 0 <= i + step * distance < count]
        arrived = jax.tree.map(lambda part: lax.ppermute(part, axis, pairs), partial)
        gathered = arrived if gathered is None else join(arrived, gathered)
        if distance * 2 < count:
            partial = join(arrived, partial)
        distance *= 2
    if gathered is None:
        gathered = jax.tree.map(jnp.zeros_like, value)
    return gathered


def gathered_in(total, state, axis):
    count, mine = lax.axis_size(axis), lax.axis_index(axis)
    packed = lax.all_gather(pack_state(total, state), axis)
    rows = state.shape[1]
    totals, states = packed[:, :, rows, 0], packed[:, :, :rows]
    place = jnp.arange(count)
    between = (place[None, :] > place[:, None]) & (place[None, :] < mine)
    span = jnp.sum(jnp.where(between[:, :, None], totals[None, :, :], 0.0), axis=1)
    factor = jnp.where((place < mine)[:, None], jnp.exp(span), 0.0)
    return jnp.einsum("jh,jhde->hde", factor, states, precision=lax.Precision.HIGHEST)


def decay_weights(cumulate, lower_mask):
    spread = cumulate.T[:, :, None] - cumulate.T[:, None, :]
    return jnp.where(lower_mask, jnp.exp(jnp.where(lower_mask, spread, 0.0)), 0.0)


def chain_join(earlier, later):
    return (earlier[0] + later[0], jnp.exp(later[0])[:, None, None] * earlier[1] + later[1])


def pack_state(total, state):
    slab = jnp.broadcast_to(total[:, None, None], (state.shape[0], 8, state.shape[2]))
    return jnp.concatenate([state, slab], axis=1)


def packed_join(earlier, later):
    rows = earlier.shape[1] - 8
    joined = chain_join((earlier[:, rows, 0], earlier[:, :rows]), (later[:, rows, 0], later[:, :rows]))
    return pack_state(*joined)


def on_device(query, keys, values, upstream, out_weight, log_decay, signs, magnitude):
    tokens = query.shape[1]
    width = query.shape[2]
    scale = HD ** (-0.5)

    def to_heads(array):
        return array.reshape(tokens, LOCAL_HEADS, HD)

    decay_here = log_decay[0]
    running = jnp.cumsum(decay_here, axis=0)
    total = running[-1]
    growth = jnp.exp(running)[:, :, None]
    remain = jnp.exp(total[None, :] - running)[:, :, None]
    query_heads = to_heads(query[0])
    key_heads = to_heads(keys[0])
    value_heads = to_heads(values[0])
    query_f32 = query_heads.astype(jnp.float32)
    key_f32 = key_heads.astype(jnp.float32)
    value_f32 = value_heads.astype(jnp.float32)

    state_end = jnp.einsum(
        "shd,she->hde", key_f32 * remain, value_f32, precision=lax.Precision.HIGHEST
    )
    split = LOCAL_HEADS // 2
    state_in = jnp.concatenate([
        carried_in(pack_state(total[:split], state_end[:split]), "ctx", packed_join, False)[:, :HD],
        gathered_in(total[split:], state_end[split:], "ctx"),
    ], axis=0)
    state_end, upstream, query_heads = lax.optimization_barrier((state_end, upstream, query_heads))

    advantage = (2 * signs[0] - 1).astype(jnp.float32) * magnitude[0]
    weighted = (advantage[:, None] * upstream[0].astype(jnp.float32)).astype(jnp.bfloat16)
    dout = lax.dot_general(
        weighted, out_weight, (((1,), (1,)), ((), ())), preferred_element_type=jnp.float32
    ).astype(jnp.bfloat16)
    dout_heads = to_heads(dout)
    dout_f32 = dout_heads.astype(jnp.float32)
    back_end = jnp.einsum(
        "thd,the->hde", query_f32 * growth, dout_f32, precision=lax.Precision.HIGHEST
    )

    lower_mask = (jnp.arange(BLOCK)[:, None] >= jnp.arange(BLOCK)[None, :])[None]
    weight = decay_weights(running, lower_mask)
    scores = jnp.einsum("thd,shd->hts", query_heads, key_heads, preferred_element_type=jnp.float32)
    probs = (scale * scores * weight).astype(jnp.bfloat16)
    attend = jnp.einsum("hts,shd->thd", probs, value_heads, preferred_element_type=jnp.float32)
    attend = attend + scale * growth * jnp.einsum(
        "thd,hde->the", query_f32, state_in, precision=lax.Precision.HIGHEST
    )
    attn = attend.reshape(tokens, width).astype(jnp.bfloat16)
    partial = lax.dot_general(
        attn, weighted, (((0,), (0,)), ((), ())), preferred_element_type=jnp.float32
    )
    partial, back_end = lax.optimization_barrier((partial, back_end))
    grad_weight = lax.psum_scatter(partial, ("ctx", "dp"), scatter_dimension=0, tiled=True)
    back_in = carried_in(pack_state(total, back_end), "ctx", packed_join, True)[:, :HD]

    dscores = jnp.einsum(
        "thd,shd->hts", dout_heads, value_heads, preferred_element_type=jnp.float32
    )
    dprobs = (scale * dscores * weight).astype(jnp.bfloat16)
    grad_q = jnp.einsum("hts,shd->thd", dprobs, key_heads, preferred_element_type=jnp.float32)
    grad_k = jnp.einsum("hts,thd->shd", dprobs, query_heads, preferred_element_type=jnp.float32)
    grad_v = jnp.einsum("hts,thd->shd", probs, dout_heads, preferred_element_type=jnp.float32)
    grad_q = grad_q + scale * growth * jnp.einsum(
        "hde,the->thd", state_in, dout_f32, precision=lax.Precision.HIGHEST
    )
    grad_k = grad_k + scale * remain * jnp.einsum(
        "hde,she->shd", back_in, value_f32, precision=lax.Precision.HIGHEST
    )
    grad_v = grad_v + scale * remain * jnp.einsum(
        "hde,shd->she", back_in, key_f32, precision=lax.Precision.HIGHEST
    )
    shape_out = (1, tokens, width)
    return (
        grad_q.reshape(shape_out).astype(jnp.bfloat16),
        grad_k.reshape(shape_out).astype(jnp.bfloat16),
        grad_v.reshape(shape_out).astype(jnp.bfloat16),
        grad_weight,
    )


def solution(mesh):
    in_specs = (
        P("dp", "ctx", None),
        P("dp", "ctx", None),
        P("dp", "ctx", None),
        P("dp", "ctx", None),
        P(),
        P("dp", "ctx", None),
        P("dp", "ctx"),
        P("dp", "ctx"),
    )
    out_specs = (
        P("dp", "ctx", None),
        P("dp", "ctx", None),
        P("dp", "ctx", None),
        P(("ctx", "dp"), None),
    )
    return jax.shard_map(
        on_device, mesh=mesh, in_specs=in_specs, out_specs=out_specs, check_vma=False
    )
```

```python
import jax
import jax.numpy as jnp
from jax import lax
from jax.sharding import PartitionSpec as P

LOCAL_HEADS = 16
HD = 128
BLOCK = 512


def carried_in(value, axis, join, backward):
    count = lax.axis_size(axis)
    step = -1 if backward else 1
    partial = value
    gathered = None
    distance = 1
    while distance < count:
        pairs = [(i, i + step * distance) for i in range(count) if 0 <= i + step * distance < count]
        arrived = jax.tree.map(lambda part: lax.ppermute(part, axis, pairs), partial)
        gathered = arrived if gathered is None else join(arrived, gathered)
        if distance * 2 < count:
            partial = join(arrived, partial)
        distance *= 2
    if gathered is None:
        gathered = jax.tree.map(jnp.zeros_like, value)
    return gathered


def split_einsum(spec, first, second):
    def passes(wide, place):
        high = wide.astype(jnp.bfloat16)
        low = (wide - high.astype(jnp.float32)).astype(jnp.bfloat16)
        out = []
        for part in (high, low):
            args = (first, part) if place == 1 else (part, second)
            out.append(jnp.einsum(spec, *args, preferred_element_type=jnp.float32))
        return out[0] + out[1]
    if first.dtype == jnp.float32:
        return passes(first, 0)
    return passes(second, 1)


def decay_weights(cumulate, lower_mask):
    spread = cumulate.T[:, :, None] - cumulate.T[:, None, :]
    return jnp.where(lower_mask, jnp.exp(jnp.where(lower_mask, spread, 0.0)), 0.0)


def chain_join(earlier, later):
    return (earlier[0] + later[0], jnp.exp(later[0])[:, None, None] * earlier[1] + later[1])


def pack_state(total, state):
    slab = jnp.broadcast_to(total[:, None, None], (state.shape[0], 8, state.shape[2]))
    return jnp.concatenate([state, slab], axis=1)


def packed_join(earlier, later):
    rows = earlier.shape[1] - 8
    joined = chain_join((earlier[:, rows, 0], earlier[:, :rows]), (later[:, rows, 0], later[:, :rows]))
    return pack_state(*joined)


def on_device(query, keys, values, upstream, out_weight, log_decay, signs, magnitude):
    tokens = query.shape[1]
    width = query.shape[2]
    scale = HD ** (-0.5)

    def to_heads(array):
        return array.reshape(tokens, LOCAL_HEADS, HD)

    decay_here = log_decay[0]
    running = jnp.cumsum(decay_here, axis=0)
    total = running[-1]
    growth = jnp.exp(running)[:, :, None]
    remain = jnp.exp(total[None, :] - running)[:, :, None]
    query_heads = to_heads(query[0])
    key_heads = to_heads(keys[0])
    value_heads = to_heads(values[0])
    query_f32 = query_heads.astype(jnp.float32)
    key_f32 = key_heads.astype(jnp.float32)
    value_f32 = value_heads.astype(jnp.float32)

    state_end = split_einsum("shd,she->hde", key_f32 * remain, value_heads)
    state_in = carried_in(pack_state(total, state_end), "ctx", packed_join, False)[:, :HD]
    state_end, upstream, query_heads = lax.optimization_barrier((state_end, upstream, query_heads))

    advantage = (2 * signs[0] - 1).astype(jnp.float32) * magnitude[0]
    weighted = (advantage[:, None] * upstream[0].astype(jnp.float32)).astype(jnp.bfloat16)
    dout = lax.dot_general(
        weighted, out_weight, (((1,), (1,)), ((), ())), preferred_element_type=jnp.float32
    ).astype(jnp.bfloat16)
    dout_heads = to_heads(dout)
    back_end = split_einsum("thd,the->hde", query_f32 * growth, dout_heads)

    lower_mask = (jnp.arange(BLOCK)[:, None] >= jnp.arange(BLOCK)[None, :])[None]
    weight = decay_weights(running, lower_mask)
    scores = jnp.einsum("thd,shd->hts", query_heads, key_heads, preferred_element_type=jnp.float32)
    probs = (scale * scores * weight).astype(jnp.bfloat16)
    attend = jnp.einsum("hts,shd->thd", probs, value_heads, preferred_element_type=jnp.float32)
    attend = attend + scale * growth * split_einsum("thd,hde->the", query_heads, state_in)
    attn = attend.reshape(tokens, width).astype(jnp.bfloat16)
    partial = lax.dot_general(
        attn, weighted, (((0,), (0,)), ((), ())), preferred_element_type=jnp.float32
    )
    partial, back_end = lax.optimization_barrier((partial, back_end))
    grad_weight = lax.psum_scatter(partial, ("ctx", "dp"), scatter_dimension=0, tiled=True)
    back_in = carried_in(pack_state(total, back_end), "ctx", packed_join, True)[:, :HD]

    dscores = jnp.einsum(
        "thd,shd->hts", dout_heads, value_heads, preferred_element_type=jnp.float32
    )
    dprobs = (scale * dscores * weight).astype(jnp.bfloat16)
    grad_q = jnp.einsum("hts,shd->thd", dprobs, key_heads, preferred_element_type=jnp.float32)
    grad_k = jnp.einsum("hts,thd->shd", dprobs, query_heads, preferred_element_type=jnp.float32)
    grad_v = jnp.einsum("hts,thd->shd", probs, dout_heads, preferred_element_type=jnp.float32)
    grad_q = grad_q + scale * growth * split_einsum("hde,the->thd", state_in, dout_heads)
    grad_k = grad_k + scale * remain * split_einsum("hde,she->shd", back_in, value_heads)
    grad_v = grad_v + scale * remain * split_einsum("hde,shd->she", back_in, key_heads)
    shape_out = (1, tokens, width)
    return (
        grad_q.reshape(shape_out).astype(jnp.bfloat16),
        grad_k.reshape(shape_out).astype(jnp.bfloat16),
        grad_v.reshape(shape_out).astype(jnp.bfloat16),
        grad_weight,
    )


def solution(mesh):
    in_specs = (
        P("dp", "ctx", None),
        P("dp", "ctx", None),
        P("dp", "ctx", None),
        P("dp", "ctx", None),
        P(),
        P("dp", "ctx", None),
        P("dp", "ctx"),
        P("dp", "ctx"),
    )
    out_specs = (
        P("dp", "ctx", None),
        P("dp", "ctx", None),
        P("dp", "ctx", None),
        P(("ctx", "dp"), None),
    )
    return jax.shard_map(
        on_device, mesh=mesh, in_specs=in_specs, out_specs=out_specs, check_vma=False
    )
```

```python
import jax
import jax.numpy as jnp
from jax import lax
from jax.sharding import PartitionSpec as P

LOCAL_HEADS = 16
HD = 128
BLOCK = 512


def carried_in(value, join, heading):
    count, groups = lax.axis_size("ctx"), lax.axis_size("dp")
    partial = value
    gathered = None
    distance = 1
    while distance < count:
        pairs = []
        for place in range(count):
            for group in range(groups):
                step = heading[group % 2] * distance
                if step != 0 and 0 <= place + step < count:
                    pairs.append((place * groups + group, (place + step) * groups + group))
        arrived = lax.ppermute(partial, ("ctx", "dp"), pairs)
        gathered = arrived if gathered is None else join(arrived, gathered)
        if distance * 2 < count:
            partial = join(arrived, partial)
        distance *= 2
    if gathered is None:
        gathered = jnp.zeros_like(value)
    return gathered


def decay_weights(cumulate, lower_mask):
    spread = cumulate.T[:, :, None] - cumulate.T[:, None, :]
    return jnp.where(lower_mask, jnp.exp(jnp.where(lower_mask, spread, 0.0)), 0.0)


def chain_join(earlier, later):
    return (earlier[0] + later[0], jnp.exp(later[0])[:, None, None] * earlier[1] + later[1])


def pack_state(total, state):
    slab = jnp.broadcast_to(total[:, None, None], (state.shape[0], 8, state.shape[2]))
    return jnp.concatenate([state, slab], axis=1)


def packed_join(earlier, later):
    rows = earlier.shape[1] - 8
    joined = chain_join((earlier[:, rows, 0], earlier[:, :rows]), (later[:, rows, 0], later[:, :rows]))
    return pack_state(*joined)


def on_device(query, keys, values, upstream, out_weight, log_decay, signs, magnitude):
    tokens = query.shape[1]
    width = query.shape[2]
    scale = HD ** (-0.5)

    def to_heads(array):
        return array.reshape(tokens, LOCAL_HEADS, HD)

    decay_here = log_decay[0]
    running = jnp.cumsum(decay_here, axis=0)
    total = running[-1]
    growth = jnp.exp(running)[:, :, None]
    remain = jnp.exp(total[None, :] - running)[:, :, None]
    query_heads = to_heads(query[0])
    key_heads = to_heads(keys[0])
    value_heads = to_heads(values[0])
    query_f32 = query_heads.astype(jnp.float32)
    key_f32 = key_heads.astype(jnp.float32)
    value_f32 = value_heads.astype(jnp.float32)

    state_end = jnp.einsum(
        "shd,she->hde", key_f32 * remain, value_f32, precision=lax.Precision.HIGHEST
    )
    state_end, upstream, query_heads = lax.optimization_barrier((state_end, upstream, query_heads))

    advantage = (2 * signs[0] - 1).astype(jnp.float32) * magnitude[0]
    weighted = (advantage[:, None] * upstream[0].astype(jnp.float32)).astype(jnp.bfloat16)
    dout = lax.dot_general(
        weighted, out_weight, (((1,), (1,)), ((), ())), preferred_element_type=jnp.float32
    ).astype(jnp.bfloat16)
    dout_heads = to_heads(dout)
    dout_f32 = dout_heads.astype(jnp.float32)
    back_end = jnp.einsum(
        "thd,the->hde", query_f32 * growth, dout_f32, precision=lax.Precision.HIGHEST
    )
    even = lax.axis_index("dp") % 2 == 0
    first = carried_in(
        pack_state(total, jnp.where(even, state_end, back_end)), packed_join, (1, -1)
    )[:, :HD]
    state_end, first = lax.optimization_barrier((state_end, first))
    second = carried_in(pack_state(total, state_end), packed_join, (0, 1))[:, :HD]
    state_in = jnp.where(even, first, second)

    lower_mask = (jnp.arange(BLOCK)[:, None] >= jnp.arange(BLOCK)[None, :])[None]
    weight = decay_weights(running, lower_mask)
    scores = jnp.einsum("thd,shd->hts", query_heads, key_heads, preferred_element_type=jnp.float32)
    probs = (scale * scores * weight).astype(jnp.bfloat16)
    attend = jnp.einsum("hts,shd->thd", probs, value_heads, preferred_element_type=jnp.float32)
    attend = attend + scale * growth * jnp.einsum(
        "thd,hde->the", query_f32, state_in, precision=lax.Precision.HIGHEST
    )
    attn = attend.reshape(tokens, width).astype(jnp.bfloat16)
    partial = lax.dot_general(
        attn, weighted, (((0,), (0,)), ((), ())), preferred_element_type=jnp.float32
    )
    partial, back_end = lax.optimization_barrier((partial, back_end))
    grad_weight = lax.psum_scatter(partial, ("ctx", "dp"), scatter_dimension=0, tiled=True)
    back_late = carried_in(pack_state(total, back_end), packed_join, (-1, 0))[:, :HD]
    back_in = jnp.where(even, back_late, first)

    dscores = jnp.einsum(
        "thd,shd->hts", dout_heads, value_heads, preferred_element_type=jnp.float32
    )
    dprobs = (scale * dscores * weight).astype(jnp.bfloat16)
    grad_q = jnp.einsum("hts,shd->thd", dprobs, key_heads, preferred_element_type=jnp.float32)
    grad_k = jnp.einsum("hts,thd->shd", dprobs, query_heads, preferred_element_type=jnp.float32)
    grad_v = jnp.einsum("hts,thd->shd", probs, dout_heads, preferred_element_type=jnp.float32)
    grad_q = grad_q + scale * growth * jnp.einsum(
        "hde,the->thd", state_in, dout_f32, precision=lax.Precision.HIGHEST
    )
    grad_k = grad_k + scale * remain * jnp.einsum(
        "hde,she->shd", back_in, value_f32, precision=lax.Precision.HIGHEST
    )
    grad_v = grad_v + scale * remain * jnp.einsum(
        "hde,shd->she", back_in, key_f32, precision=lax.Precision.HIGHEST
    )
    shape_out = (1, tokens, width)
    return (
        grad_q.reshape(shape_out).astype(jnp.bfloat16),
        grad_k.reshape(shape_out).astype(jnp.bfloat16),
        grad_v.reshape(shape_out).astype(jnp.bfloat16),
        grad_weight,
    )


def solution(mesh):
    in_specs = (
        P("dp", "ctx", None),
        P("dp", "ctx", None),
        P("dp", "ctx", None),
        P("dp", "ctx", None),
        P(),
        P("dp", "ctx", None),
        P("dp", "ctx"),
        P("dp", "ctx"),
    )
    out_specs = (
        P("dp", "ctx", None),
        P("dp", "ctx", None),
        P("dp", "ctx", None),
        P(("ctx", "dp"), None),
    )
    return jax.shard_map(
        on_device, mesh=mesh, in_specs=in_specs, out_specs=out_specs, check_vma=False
    )
```

```python
import jax
import jax.numpy as jnp
from jax import lax
from jax.sharding import PartitionSpec as P

LOCAL_HEADS = 16
HD = 128
BLOCK = 512


def carried_in(value, axis, join, backward):
    count = lax.axis_size(axis)
    step = -1 if backward else 1
    partial = value
    gathered = None
    distance = 1
    while distance < count:
        pairs = [(i, i + step * distance) for i in range(count) if 0 <= i + step * distance < count]
        arrived = jax.tree.map(lambda part: lax.ppermute(part, axis, pairs), partial)
        gathered = arrived if gathered is None else join(arrived, gathered)
        if distance * 2 < count:
            partial = join(arrived, partial)
        distance *= 2
    if gathered is None:
        gathered = jax.tree.map(jnp.zeros_like, value)
    return gathered


def decay_weights(cumulate, lower_mask):
    spread = cumulate.T[:, :, None] - cumulate.T[:, None, :]
    return jnp.where(lower_mask, jnp.exp(jnp.where(lower_mask, spread, 0.0)), 0.0)


def chain_join(earlier, later):
    return (earlier[0] + later[0], jnp.exp(later[0])[:, None, None] * earlier[1] + later[1])


def pack_state(total, state):
    slab = jnp.broadcast_to(total[:, None, None], (state.shape[0], 8, state.shape[2]))
    return jnp.concatenate([state, slab], axis=1)


def packed_join(earlier, later):
    rows = earlier.shape[1] - 8
    joined = chain_join((earlier[:, rows, 0], earlier[:, :rows]), (later[:, rows, 0], later[:, :rows]))
    return pack_state(*joined)


def on_device(query, keys, values, upstream, out_weight, log_decay, signs, magnitude):
    tokens = query.shape[1]
    width = query.shape[2]
    scale = HD ** (-0.5)

    def to_heads(array):
        return array.reshape(tokens, LOCAL_HEADS, HD)

    decay_here = log_decay[0]
    running = jnp.cumsum(decay_here, axis=0)
    total = running[-1]
    growth = jnp.exp(running)[:, :, None]
    remain = jnp.exp(total[None, :] - running)[:, :, None]
    query_heads = to_heads(query[0])
    key_heads = to_heads(keys[0])
    value_heads = to_heads(values[0])
    query_f32 = query_heads.astype(jnp.float32)
    key_f32 = key_heads.astype(jnp.float32)
    value_f32 = value_heads.astype(jnp.float32)

    state_end = jnp.einsum(
        "shd,she->hde", key_f32 * remain, value_f32, precision=lax.Precision.HIGH
    )
    state_in = carried_in(pack_state(total, state_end), "ctx", packed_join, False)[:, :HD]
    state_end, upstream, query_heads = lax.optimization_barrier((state_end, upstream, query_heads))

    advantage = (2 * signs[0] - 1).astype(jnp.float32) * magnitude[0]
    weighted = (advantage[:, None] * upstream[0].astype(jnp.float32)).astype(jnp.bfloat16)
    dout = lax.dot_general(
        weighted, out_weight, (((1,), (1,)), ((), ())), preferred_element_type=jnp.float32
    ).astype(jnp.bfloat16)
    dout_heads = to_heads(dout)
    dout_f32 = dout_heads.astype(jnp.float32)
    back_end = jnp.einsum(
        "thd,the->hde", query_f32 * growth, dout_f32, precision=lax.Precision.HIGH
    )

    lower_mask = (jnp.arange(BLOCK)[:, None] >= jnp.arange(BLOCK)[None, :])[None]
    weight = decay_weights(running, lower_mask)
    scores = jnp.einsum("thd,shd->hts", query_heads, key_heads, preferred_element_type=jnp.float32)
    probs = (scale * scores * weight).astype(jnp.bfloat16)
    attend = jnp.einsum("hts,shd->thd", probs, value_heads, preferred_element_type=jnp.float32)
    attend = attend + scale * growth * jnp.einsum(
        "thd,hde->the", query_f32, state_in, precision=lax.Precision.HIGH
    )
    attn = attend.reshape(tokens, width).astype(jnp.bfloat16)
    partial = lax.dot_general(
        attn, weighted, (((0,), (0,)), ((), ())), preferred_element_type=jnp.float32
    )
    partial, back_end = lax.optimization_barrier((partial, back_end))
    grad_weight = lax.psum_scatter(partial, ("ctx", "dp"), scatter_dimension=0, tiled=True)
    back_in = carried_in(pack_state(total, back_end), "ctx", packed_join, True)[:, :HD]

    dscores = jnp.einsum(
        "thd,shd->hts", dout_heads, value_heads, preferred_element_type=jnp.float32
    )
    dprobs = (scale * dscores * weight).astype(jnp.bfloat16)
    grad_q = jnp.einsum("hts,shd->thd", dprobs, key_heads, preferred_element_type=jnp.float32)
    grad_k = jnp.einsum("hts,thd->shd", dprobs, query_heads, preferred_element_type=jnp.float32)
    grad_v = jnp.einsum("hts,thd->shd", probs, dout_heads, preferred_element_type=jnp.float32)
    grad_q = grad_q + scale * growth * jnp.einsum(
        "hde,the->thd", state_in, dout_f32, precision=lax.Precision.HIGH
    )
    grad_k = grad_k + scale * remain * jnp.einsum(
        "hde,she->shd", back_in, value_f32, precision=lax.Precision.HIGH
    )
    grad_v = grad_v + scale * remain * jnp.einsum(
        "hde,shd->she", back_in, key_f32, precision=lax.Precision.HIGH
    )
    shape_out = (1, tokens, width)
    return (
        grad_q.reshape(shape_out).astype(jnp.bfloat16),
        grad_k.reshape(shape_out).astype(jnp.bfloat16),
        grad_v.reshape(shape_out).astype(jnp.bfloat16),
        grad_weight,
    )


def solution(mesh):
    in_specs = (
        P("dp", "ctx", None),
        P("dp", "ctx", None),
        P("dp", "ctx", None),
        P("dp", "ctx", None),
        P(),
        P("dp", "ctx", None),
        P("dp", "ctx"),
        P("dp", "ctx"),
    )
    out_specs = (
        P("dp", "ctx", None),
        P("dp", "ctx", None),
        P("dp", "ctx", None),
        P(("ctx", "dp"), None),
    )
    return jax.shard_map(
        on_device, mesh=mesh, in_specs=in_specs, out_specs=out_specs, check_vma=False
    )
```

```python
import jax
import jax.numpy as jnp
from jax import lax
from jax.sharding import PartitionSpec as P

LOCAL_HEADS = 16
HD = 128
BLOCK = 512


def carried_in(value, axis, join, backward):
    count = lax.axis_size(axis)
    step = -1 if backward else 1
    partial = value
    gathered = None
    distance = 1
    while distance < count:
        pairs = [(i, i + step * distance) for i in range(count) if 0 <= i + step * distance < count]
        arrived = jax.tree.map(lambda part: lax.ppermute(part, axis, pairs), partial)
        gathered = arrived if gathered is None else join(arrived, gathered)
        if distance * 2 < count:
            partial = join(arrived, partial)
        distance *= 2
    if gathered is None:
        gathered = jax.tree.map(jnp.zeros_like, value)
    return gathered


def carried_groups(value, join, heading):
    count, groups = lax.axis_size("ctx"), lax.axis_size("dp")
    partial = value
    gathered = None
    distance = 1
    while distance < count:
        pairs = []
        for place in range(count):
            for group in range(groups):
                step = heading[group % 2] * distance
                if step != 0 and 0 <= place + step < count:
                    pairs.append((place * groups + group, (place + step) * groups + group))
        arrived = lax.ppermute(partial, ("ctx", "dp"), pairs)
        gathered = arrived if gathered is None else join(arrived, gathered)
        if distance * 2 < count:
            partial = join(arrived, partial)
        distance *= 2
    if gathered is None:
        gathered = jnp.zeros_like(value)
    return gathered


def decay_weights(cumulate, lower_mask):
    spread = cumulate.T[:, :, None] - cumulate.T[:, None, :]
    return jnp.where(lower_mask, jnp.exp(jnp.where(lower_mask, spread, 0.0)), 0.0)


def chain_join(earlier, later):
    return (earlier[0] + later[0], jnp.exp(later[0])[:, None, None] * earlier[1] + later[1])


def pack_state(total, state):
    slab = jnp.broadcast_to(total[:, None, None], (state.shape[0], 8, state.shape[2]))
    return jnp.concatenate([state, slab], axis=1)


def packed_join(earlier, later):
    rows = earlier.shape[1] - 8
    joined = chain_join((earlier[:, rows, 0], earlier[:, :rows]), (later[:, rows, 0], later[:, :rows]))
    return pack_state(*joined)


def on_device(query, keys, values, upstream, out_weight, log_decay, signs, magnitude):
    tokens = query.shape[1]
    width = query.shape[2]
    scale = HD ** (-0.5)

    def to_heads(array):
        return array.reshape(tokens, LOCAL_HEADS, HD)

    decay_here = log_decay[0]
    running = jnp.cumsum(decay_here, axis=0)
    total = running[-1]
    growth = jnp.exp(running)[:, :, None]
    remain = jnp.exp(total[None, :] - running)[:, :, None]
    query_heads = to_heads(query[0])
    key_heads = to_heads(keys[0])
    value_heads = to_heads(values[0])
    query_f32 = query_heads.astype(jnp.float32)
    key_f32 = key_heads.astype(jnp.float32)
    value_f32 = value_heads.astype(jnp.float32)

    state_end = jnp.einsum(
        "shd,she->hde", key_f32 * remain, value_f32, precision=lax.Precision.HIGH
    )
    state_in = carried_in(pack_state(total, state_end), "ctx", packed_join, False)[:, :HD]
    state_end, upstream, query_heads = lax.optimization_barrier((state_end, upstream, query_heads))

    advantage = (2 * signs[0] - 1).astype(jnp.float32) * magnitude[0]
    weighted = (advantage[:, None] * upstream[0].astype(jnp.float32)).astype(jnp.bfloat16)
    dout = lax.dot_general(
        weighted, out_weight, (((1,), (1,)), ((), ())), preferred_element_type=jnp.float32
    ).astype(jnp.bfloat16)
    dout_heads = to_heads(dout)
    dout_f32 = dout_heads.astype(jnp.float32)
    back_end = jnp.einsum(
        "thd,the->hde", query_f32 * growth, dout_f32, precision=lax.Precision.HIGH
    )

    lower_mask = (jnp.arange(BLOCK)[:, None] >= jnp.arange(BLOCK)[None, :])[None]
    weight = decay_weights(running, lower_mask)
    scores = jnp.einsum("thd,shd->hts", query_heads, key_heads, preferred_element_type=jnp.float32)
    probs = (scale * scores * weight).astype(jnp.bfloat16)
    attend = jnp.einsum("hts,shd->thd", probs, value_heads, preferred_element_type=jnp.float32)
    attend = attend + scale * growth * jnp.einsum(
        "thd,hde->the", query_f32, state_in, precision=lax.Precision.HIGH
    )
    attn = attend.reshape(tokens, width).astype(jnp.bfloat16)
    partial = lax.dot_general(
        attn, weighted, (((0,), (0,)), ((), ())), preferred_element_type=jnp.float32
    )
    partial, back_end = lax.optimization_barrier((partial, back_end))
    grad_weight = lax.psum_scatter(partial, ("ctx", "dp"), scatter_dimension=0, tiled=True)
    even = lax.axis_index("dp") % 2 == 0
    back_even = carried_groups(pack_state(total, back_end), packed_join, (-1, 0))[:, :HD]
    back_end, back_even = lax.optimization_barrier((back_end, back_even))
    back_odd = carried_groups(pack_state(total, back_end), packed_join, (0, -1))[:, :HD]
    back_in = jnp.where(even, back_even, back_odd)

    dscores = jnp.einsum(
        "thd,shd->hts", dout_heads, value_heads, preferred_element_type=jnp.float32
    )
    dprobs = (scale * dscores * weight).astype(jnp.bfloat16)
    grad_q = jnp.einsum("hts,shd->thd", dprobs, key_heads, preferred_element_type=jnp.float32)
    grad_k = jnp.einsum("hts,thd->shd", dprobs, query_heads, preferred_element_type=jnp.float32)
    grad_v = jnp.einsum("hts,thd->shd", probs, dout_heads, preferred_element_type=jnp.float32)
    grad_q = grad_q + scale * growth * jnp.einsum(
        "hde,the->thd", state_in, dout_f32, precision=lax.Precision.HIGH
    )
    grad_k = grad_k + scale * remain * jnp.einsum(
        "hde,she->shd", back_in, value_f32, precision=lax.Precision.HIGH
    )
    grad_v = grad_v + scale * remain * jnp.einsum(
        "hde,shd->she", back_in, key_f32, precision=lax.Precision.HIGH
    )
    shape_out = (1, tokens, width)
    return (
        grad_q.reshape(shape_out).astype(jnp.bfloat16),
        grad_k.reshape(shape_out).astype(jnp.bfloat16),
        grad_v.reshape(shape_out).astype(jnp.bfloat16),
        grad_weight,
    )


def solution(mesh):
    in_specs = (
        P("dp", "ctx", None),
        P("dp", "ctx", None),
        P("dp", "ctx", None),
        P("dp", "ctx", None),
        P(),
        P("dp", "ctx", None),
        P("dp", "ctx"),
        P("dp", "ctx"),
    )
    out_specs = (
        P("dp", "ctx", None),
        P("dp", "ctx", None),
        P("dp", "ctx", None),
        P(("ctx", "dp"), None),
    )
    return jax.shard_map(
        on_device, mesh=mesh, in_specs=in_specs, out_specs=out_specs, check_vma=False
    )
```

```python
import jax
import jax.numpy as jnp
from jax import lax
from jax.sharding import PartitionSpec as P

LOCAL_HEADS = 16
HD = 128
BLOCK = 512


def carried_in(value, axis, join, backward):
    count = lax.axis_size(axis)
    step = -1 if backward else 1
    partial = value
    gathered = None
    distance = 1
    while distance < count:
        pairs = [(i, i + step * distance) for i in range(count) if 0 <= i + step * distance < count]
        arrived = jax.tree.map(lambda part: lax.ppermute(part, axis, pairs), partial)
        gathered = arrived if gathered is None else join(arrived, gathered)
        if distance * 2 < count:
            partial = join(arrived, partial)
        distance *= 2
    if gathered is None:
        gathered = jax.tree.map(jnp.zeros_like, value)
    return gathered


def decay_weights(cumulate, lower_mask):
    spread = cumulate.T[:, :, None] - cumulate.T[:, None, :]
    return jnp.where(lower_mask, jnp.exp(jnp.where(lower_mask, spread, 0.0)), 0.0)


def chain_join(earlier, later):
    return (earlier[0] + later[0], jnp.exp(later[0])[:, None, None] * earlier[1] + later[1])


def pack_state(total, state):
    slab = jnp.broadcast_to(total[:, None, None], (state.shape[0], 8, state.shape[2]))
    return jnp.concatenate([state, slab], axis=1)


def packed_join(earlier, later):
    rows = earlier.shape[1] - 8
    joined = chain_join((earlier[:, rows, 0], earlier[:, :rows]), (later[:, rows, 0], later[:, :rows]))
    return pack_state(*joined)


def on_device(query, keys, values, upstream, out_weight, log_decay, signs, magnitude):
    tokens = query.shape[1]
    width = query.shape[2]
    scale = HD ** (-0.5)

    def to_heads(array):
        return array.reshape(tokens, LOCAL_HEADS, HD)

    decay_here = log_decay[0]
    running = jnp.cumsum(decay_here, axis=0)
    total = running[-1]
    growth = jnp.exp(running)[:, :, None]
    remain = jnp.exp(total[None, :] - running)[:, :, None]
    query_heads = to_heads(query[0])
    key_heads = to_heads(keys[0])
    value_heads = to_heads(values[0])
    query_f32 = query_heads.astype(jnp.float32)
    key_f32 = key_heads.astype(jnp.float32)
    value_f32 = value_heads.astype(jnp.float32)

    state_end = jnp.einsum(
        "shd,she->hde", key_f32 * remain, value_f32, precision=lax.Precision.HIGH
    )
    state_in = carried_in(pack_state(total, state_end), "ctx", packed_join, False)[:, :HD]

    advantage = (2 * signs[0] - 1).astype(jnp.float32) * magnitude[0]
    weighted = (advantage[:, None] * upstream[0].astype(jnp.float32)).astype(jnp.bfloat16)
    dout = lax.dot_general(
        weighted, out_weight, (((1,), (1,)), ((), ())), preferred_element_type=jnp.float32
    ).astype(jnp.bfloat16)
    dout_heads = to_heads(dout)
    dout_f32 = dout_heads.astype(jnp.float32)
    back_end = jnp.einsum(
        "thd,the->hde", query_f32 * growth, dout_f32, precision=lax.Precision.HIGH
    )

    lower_mask = (jnp.arange(BLOCK)[:, None] >= jnp.arange(BLOCK)[None, :])[None]
    weight = decay_weights(running, lower_mask)
    scores = jnp.einsum("thd,shd->hts", query_heads, key_heads, preferred_element_type=jnp.float32)
    probs = (scale * scores * weight).astype(jnp.bfloat16)
    attend = jnp.einsum("hts,shd->thd", probs, value_heads, preferred_element_type=jnp.float32)
    attend = attend + scale * growth * jnp.einsum(
        "thd,hde->the", query_f32, state_in, precision=lax.Precision.HIGH
    )
    attn = attend.reshape(tokens, width).astype(jnp.bfloat16)
    partial = lax.dot_general(
        attn, weighted, (((0,), (0,)), ((), ())), preferred_element_type=jnp.float32
    )
    partial, back_end = lax.optimization_barrier((partial, back_end))
    grad_weight = lax.psum_scatter(partial, ("ctx", "dp"), scatter_dimension=0, tiled=True)
    back_in = carried_in(pack_state(total, back_end), "ctx", packed_join, True)[:, :HD]

    dscores = jnp.einsum(
        "thd,shd->hts", dout_heads, value_heads, preferred_element_type=jnp.float32
    )
    dprobs = (scale * dscores * weight).astype(jnp.bfloat16)
    grad_q = jnp.einsum("hts,shd->thd", dprobs, key_heads, preferred_element_type=jnp.float32)
    grad_k = jnp.einsum("hts,thd->shd", dprobs, query_heads, preferred_element_type=jnp.float32)
    grad_v = jnp.einsum("hts,thd->shd", probs, dout_heads, preferred_element_type=jnp.float32)
    grad_q = grad_q + scale * growth * jnp.einsum(
        "hde,the->thd", state_in, dout_f32, precision=lax.Precision.HIGH
    )
    grad_k = grad_k + scale * remain * jnp.einsum(
        "hde,she->shd", back_in, value_f32, precision=lax.Precision.HIGH
    )
    grad_v = grad_v + scale * remain * jnp.einsum(
        "hde,shd->she", back_in, key_f32, precision=lax.Precision.HIGH
    )
    shape_out = (1, tokens, width)
    return (
        grad_q.reshape(shape_out).astype(jnp.bfloat16),
        grad_k.reshape(shape_out).astype(jnp.bfloat16),
        grad_v.reshape(shape_out).astype(jnp.bfloat16),
        grad_weight,
    )


def solution(mesh):
    in_specs = (
        P("dp", "ctx", None),
        P("dp", "ctx", None),
        P("dp", "ctx", None),
        P("dp", "ctx", None),
        P(),
        P("dp", "ctx", None),
        P("dp", "ctx"),
        P("dp", "ctx"),
    )
    out_specs = (
        P("dp", "ctx", None),
        P("dp", "ctx", None),
        P("dp", "ctx", None),
        P(("ctx", "dp"), None),
    )
    return jax.shard_map(
        on_device, mesh=mesh, in_specs=in_specs, out_specs=out_specs, check_vma=False
    )
```

```python
import jax
import jax.numpy as jnp
from jax import lax
from jax.sharding import PartitionSpec as P

LOCAL_HEADS = 16
HD = 128
BLOCK = 512


def carried_in(value, axis, join, backward):
    count = lax.axis_size(axis)
    step = -1 if backward else 1
    partial = value
    gathered = None
    distance = 1
    while distance < count:
        pairs = [(i, i + step * distance) for i in range(count) if 0 <= i + step * distance < count]
        if distance * 2 < count:
            arrived = lax.ppermute(partial, axis, pairs)
        else:
            rows = partial.shape[1] - 8
            arrived = lax.ppermute(partial[:, :rows], axis, pairs)
            arrived = jnp.concatenate([arrived, jnp.zeros_like(partial[:, rows:])], axis=1)
        gathered = arrived if gathered is None else join(arrived, gathered)
        if distance * 2 < count:
            partial = join(arrived, partial)
        distance *= 2
    if gathered is None:
        gathered = jax.tree.map(jnp.zeros_like, value)
    return gathered


def decay_weights(cumulate, lower_mask):
    spread = cumulate.T[:, :, None] - cumulate.T[:, None, :]
    return jnp.where(lower_mask, jnp.exp(jnp.where(lower_mask, spread, 0.0)), 0.0)


def chain_join(earlier, later):
    return (earlier[0] + later[0], jnp.exp(later[0])[:, None, None] * earlier[1] + later[1])


def pack_state(total, state):
    slab = jnp.broadcast_to(total[:, None, None], (state.shape[0], 8, state.shape[2]))
    return jnp.concatenate([state, slab], axis=1)


def packed_join(earlier, later):
    rows = earlier.shape[1] - 8
    joined = chain_join((earlier[:, rows, 0], earlier[:, :rows]), (later[:, rows, 0], later[:, :rows]))
    return pack_state(*joined)


def on_device(query, keys, values, upstream, out_weight, log_decay, signs, magnitude):
    tokens = query.shape[1]
    width = query.shape[2]
    scale = HD ** (-0.5)

    def to_heads(array):
        return array.reshape(tokens, LOCAL_HEADS, HD)

    decay_here = log_decay[0]
    running = jnp.cumsum(decay_here, axis=0)
    total = running[-1]
    growth = jnp.exp(running)[:, :, None]
    remain = jnp.exp(total[None, :] - running)[:, :, None]
    query_heads = to_heads(query[0])
    key_heads = to_heads(keys[0])
    value_heads = to_heads(values[0])
    query_f32 = query_heads.astype(jnp.float32)
    key_f32 = key_heads.astype(jnp.float32)
    value_f32 = value_heads.astype(jnp.float32)

    state_end = jnp.einsum(
        "shd,she->hde", key_f32 * remain, value_f32, precision=lax.Precision.HIGH
    )
    state_in = carried_in(pack_state(total, state_end), "ctx", packed_join, False)[:, :HD]
    state_end, upstream, query_heads = lax.optimization_barrier((state_end, upstream, query_heads))

    advantage = (2 * signs[0] - 1).astype(jnp.float32) * magnitude[0]
    weighted = (advantage[:, None] * upstream[0].astype(jnp.float32)).astype(jnp.bfloat16)
    dout = lax.dot_general(
        weighted, out_weight, (((1,), (1,)), ((), ())), preferred_element_type=jnp.float32
    ).astype(jnp.bfloat16)
    dout_heads = to_heads(dout)
    dout_f32 = dout_heads.astype(jnp.float32)
    back_end = jnp.einsum(
        "thd,the->hde", query_f32 * growth, dout_f32, precision=lax.Precision.HIGH
    )

    lower_mask = (jnp.arange(BLOCK)[:, None] >= jnp.arange(BLOCK)[None, :])[None]
    weight = decay_weights(running, lower_mask)
    scores = jnp.einsum("thd,shd->hts", query_heads, key_heads, preferred_element_type=jnp.float32)
    probs = (scale * scores * weight).astype(jnp.bfloat16)
    attend = jnp.einsum("hts,shd->thd", probs, value_heads, preferred_element_type=jnp.float32)
    attend = attend + scale * growth * jnp.einsum(
        "thd,hde->the", query_f32, state_in, precision=lax.Precision.HIGH
    )
    attn = attend.reshape(tokens, width).astype(jnp.bfloat16)
    partial = lax.dot_general(
        attn, weighted, (((0,), (0,)), ((), ())), preferred_element_type=jnp.float32
    )
    partial, back_end = lax.optimization_barrier((partial, back_end))
    grad_weight = lax.psum_scatter(partial, ("ctx", "dp"), scatter_dimension=0, tiled=True)
    back_in = carried_in(pack_state(total, back_end), "ctx", packed_join, True)[:, :HD]

    dscores = jnp.einsum(
        "thd,shd->hts", dout_heads, value_heads, preferred_element_type=jnp.float32
    )
    dprobs = (scale * dscores * weight).astype(jnp.bfloat16)
    grad_q = jnp.einsum("hts,shd->thd", dprobs, key_heads, preferred_element_type=jnp.float32)
    grad_k = jnp.einsum("hts,thd->shd", dprobs, query_heads, preferred_element_type=jnp.float32)
    grad_v = jnp.einsum("hts,thd->shd", probs, dout_heads, preferred_element_type=jnp.float32)
    grad_q = grad_q + scale * growth * jnp.einsum(
        "hde,the->thd", state_in, dout_f32, precision=lax.Precision.HIGH
    )
    grad_k = grad_k + scale * remain * jnp.einsum(
        "hde,she->shd", back_in, value_f32, precision=lax.Precision.HIGH
    )
    grad_v = grad_v + scale * remain * jnp.einsum(
        "hde,shd->she", back_in, key_f32, precision=lax.Precision.HIGH
    )
    shape_out = (1, tokens, width)
    return (
        grad_q.reshape(shape_out).astype(jnp.bfloat16),
        grad_k.reshape(shape_out).astype(jnp.bfloat16),
        grad_v.reshape(shape_out).astype(jnp.bfloat16),
        grad_weight,
    )


def solution(mesh):
    in_specs = (
        P("dp", "ctx", None),
        P("dp", "ctx", None),
        P("dp", "ctx", None),
        P("dp", "ctx", None),
        P(),
        P("dp", "ctx", None),
        P("dp", "ctx"),
        P("dp", "ctx"),
    )
    out_specs = (
        P("dp", "ctx", None),
        P("dp", "ctx", None),
        P("dp", "ctx", None),
        P(("ctx", "dp"), None),
    )
    return jax.shard_map(
        on_device, mesh=mesh, in_specs=in_specs, out_specs=out_specs, check_vma=False
    )
```
